256 devices in a mesh: grp: 16 (over z, core), seq: 16 (over y, x).
Axes of the slice: x: 4, y: 4, z: 8, core: 2. Of those that a mesh axis runs over, the one named last changes fastest.
Arguments:
- query: bfloat16 [32, 8192], P('grp', 'seq'), may hold values from -16 to 16
- key_cache: bfloat16 [32, 16384, 1024], P('grp', 'seq'), may hold values from -64 to 64
- value_store_cache: bfloat16 [32, 16384, 1024], P('grp', 'seq'), may hold values from -6 to 6
- selected: int32 [32, 32], P('grp'), may hold values from 0 to 255, as said below
- lengths: int32 [32], P('grp'), may hold values from 2048 to 16384, as said below
- w_out: bfloat16 [8192, 8192], P('seq', 'grp'), may hold values from -0.0625 to 0.0625
Outputs:
- attended: bfloat16 [32, 8192], P('grp', 'seq')
- projected: bfloat16 [32, 8192], P('seq', 'grp')
The draws below stay inside these ranges and needn't reach their ends.
Inputs may be any that keep to these rules, and one draw needn't show every extreme that they name: `selected`: each row lists 32 distinct page numbers in ascending order, all below ceil(lengths / 64), always including the page that holds position lengths - 1; recent pages are chosen more often. `lengths`: every length is at least 2048; some request has exactly 16384.
All inputs are finite; a program needn't handle non-finite values.
Results may differ from the reference program's by a relative error of at most 0.0056.
Values may be sent and summed in bfloat16 or wider, within the bound.
No kernel may reach another device: no remote copies, remote signals or barrier semaphores. Data moves between devices by JAX's collectives and lax.ppermute only.
A program may use at most 64 MiB of HBM per device.

```python
import jax
import jax.numpy as jnp
from jax import lax

QUERY_HEADS = 64
KEY_VALUE_HEADS = 8
HEAD_DIMENSION = 128
D = 8192
PAGE = 64
SEL = 32
PG_DEV = 16
TOTAL_REQUESTS = 32
REQUEST_PAGES = 256
CACHE_SPAN = 16384
N_SEQ = 16


def length_draw(key):
    lowest = SEL * PAGE
    drawn = CACHE_SPAN - jax.random.randint(jax.random.fold_in(key, 11), (TOTAL_REQUESTS,), 0, CACHE_SPAN - lowest + 1)
    drawn = jnp.where(drawn % PAGE == 1, drawn + 1, drawn)
    drawn = jnp.where(jnp.arange(TOTAL_REQUESTS) == 0, CACHE_SPAN, drawn)
    return drawn.astype(jnp.int32)


def draw_lengths(key, part):
    return length_draw(key)


def draw_selected(key, part):
    lengths = length_draw(key)
    page_count = (lengths + PAGE - 1) // PAGE
    page_number = jnp.arange(REQUEST_PAGES).astype(jnp.int32)[None, :]
    base_offset = jax.random.randint(jax.random.fold_in(key, 12), (TOTAL_REQUESTS, REQUEST_PAGES), 0, 2 ** 18)
    extra_score = jnp.where(page_number * 4 >= page_count[:, None] * 3, 2 ** 15, 0)
    value_entry = (base_offset + extra_score) * REQUEST_PAGES + page_number
    value_entry = jnp.where(page_number == page_count[:, None] - 1, 2 ** 30, value_entry)
    value_entry = jnp.where(page_number < page_count[:, None], value_entry, -1 - page_number)
    picked = lax.top_k(value_entry, SEL)[1]
    return jnp.sort(picked, axis=1).astype(jnp.int32)


def draw_query(key, part):
    head_group = QUERY_HEADS // KEY_VALUE_HEADS
    base_offset = jnp.clip(jax.random.normal(jax.random.fold_in(key, 1), (TOTAL_REQUESTS, KEY_VALUE_HEADS, head_group, HEAD_DIMENSION), jnp.float32), -6.0, 6.0)
    return base_offset.reshape(TOTAL_REQUESTS, QUERY_HEADS * HEAD_DIMENSION).astype(jnp.bfloat16)


def draw_key_cache(key, part):
    base_offset = jnp.clip(jax.random.normal(jax.random.fold_in(key, 2), (TOTAL_REQUESTS, CACHE_SPAN, KEY_VALUE_HEADS, HEAD_DIMENSION), jnp.float32), -6.0, 6.0)
    return base_offset.reshape(TOTAL_REQUESTS, CACHE_SPAN, KEY_VALUE_HEADS * HEAD_DIMENSION).astype(jnp.bfloat16)


def block_scale(rng, extent, shards, smallest, high):
    gain, own = 1.0, jax.random.fold_in(rng, 6)
    for axis_at, blocks in shards:
        heights = jnp.exp(jax.random.uniform(jax.random.fold_in(own, axis_at), (blocks,), jnp.float32, smallest / len(shards), high / len(shards)))
        gain = gain * jnp.repeat(heights, extent[axis_at] // blocks).reshape([-1 if axis == axis_at else 1 for axis in range(len(extent))])
    return gain


def bell_draw(stream_key, shape, scale, bound, pieces=(), dtype=jnp.bfloat16):
    level = block_scale(stream_key, shape, pieces, -0.22, 0.18) if pieces else 1.0
    values = jax.random.normal(stream_key, shape, jnp.float32) * scale * level
    return jnp.minimum(jnp.maximum(values, -bound), bound).astype(dtype)


def setup_inputs(seed: int = 0) -> dict:
    arg_keys = jax.random.split(jax.random.key(seed), 7)
    return {
        "query": draw_query(jax.random.fold_in(arg_keys[6], 71), 0),
        "key_cache": draw_key_cache(jax.random.fold_in(arg_keys[6], 71), 0),
        "value_store_cache": bell_draw(arg_keys[2], (TOTAL_REQUESTS, CACHE_SPAN, KEY_VALUE_HEADS * HEAD_DIMENSION), 1.0, 6.0, ((0, 16), (1, 16))),
        "selected": draw_selected(jax.random.fold_in(arg_keys[6], 71), 0),
        "lengths": draw_lengths(jax.random.fold_in(arg_keys[6], 71), 0),
        "w_out": bell_draw(arg_keys[5], (QUERY_HEADS * HEAD_DIMENSION, D), (QUERY_HEADS * HEAD_DIMENSION) ** -0.5, 0.0625, ((0, 16), (1, 16))),
    }


NEG = -1e30


def one_request(items):
    query_row, all_key_rows, all_value_rows, sel, length = items
    head_group = QUERY_HEADS // KEY_VALUE_HEADS
    cache_position = (sel[:, None] * PAGE + jnp.arange(PAGE).astype(jnp.int32)[None, :]).reshape(-1).astype(jnp.int32)
    key_rows = jnp.take(all_key_rows, cache_position, axis=0).astype(jnp.float32).reshape(-1, KEY_VALUE_HEADS, HEAD_DIMENSION)
    value_rows = jnp.take(all_value_rows, cache_position, axis=0).astype(jnp.float32).reshape(-1, KEY_VALUE_HEADS, HEAD_DIMENSION)
    query_group = query_row.astype(jnp.float32).reshape(KEY_VALUE_HEADS, head_group, HEAD_DIMENSION)
    scores = jnp.einsum('kgd,tkd->kgt', query_group, key_rows) * (HEAD_DIMENSION ** -0.5)
    live = cache_position < length
    block = cache_position // (PG_DEV * PAGE)
    onehot = block[None, :] == jnp.arange(N_SEQ).astype(jnp.int32)[:, None]
    cand = jnp.where(onehot & live[None, :], scores[:, :, None, :], NEG)
    blockmax = jnp.max(cand, axis=-1)
    tokmax = jnp.max(jnp.where(onehot, blockmax[..., None], NEG), axis=-2)
    weight = jnp.where(live, jnp.exp(scores - tokmax), 0.0)
    weight_b = lax.optimization_barrier(weight.astype(jnp.bfloat16)).astype(jnp.float32)
    blocksum = jnp.sum(jnp.where(onehot, weight[:, :, None, :], 0.0), axis=-1)
    blockw = jnp.where(onehot, weight_b[:, :, None, :], 0.0)
    blockout = jnp.einsum('kgbt,tkd->kgbd', blockw, value_rows)
    top = jnp.max(blockmax, axis=-1)
    factor = jnp.exp(blockmax - top[..., None])
    total = jnp.sum(blocksum * factor, axis=-1)
    merged = jnp.sum(blockout * factor[..., None], axis=2)
    return (merged / total[..., None]).reshape(-1).astype(jnp.bfloat16)


def reference(query, key_cache, value_store_cache, selected, lengths, w_out):
    attended = lax.map(one_request, (query, key_cache, value_store_cache, selected, lengths))
    projected = jnp.dot(attended, w_out, preferred_element_type=jnp.float32).astype(jnp.bfloat16)
    return attended, projected
```

```python
import jax
import jax.numpy as jnp
from jax import lax
from jax.sharding import PartitionSpec as P

HEAD_DIMENSION = 128
PAGE = 64


NEG = -1e30


def gather_by_all_to_all(x, axis):
    n = lax.axis_size(axis)
    return lax.all_to_all(jnp.broadcast_to(x[None], (n,) + x.shape), axis, 0, 0, tiled=True)


def body(query, key_cache, value_store_cache, selected, lengths, w_out):
    nseq = lax.axis_size("seq")
    me = lax.axis_index("seq")
    requests = query.shape[0]
    tok_local = key_cache.shape[1]
    kv_heads = key_cache.shape[2] // HEAD_DIMENSION
    heads_dev = query.shape[1] // HEAD_DIMENSION
    q_heads = heads_dev * nseq
    head_group = q_heads // kv_heads
    scale = HEAD_DIMENSION ** (-0.5)

    heads_all = gather_by_all_to_all(query, "seq")
    qgroup = jnp.transpose(heads_all, (1, 0, 2)).reshape(requests, kv_heads, head_group, HEAD_DIMENSION)

    pages_local = tok_local // PAGE
    first_page = me * pages_local
    page_ids = first_page + jnp.arange(pages_local, dtype=jnp.int32)
    page_picked = jnp.any(selected[:, :, None] == page_ids[None, None, :], axis=1)
    positions = me * tok_local + jnp.arange(tok_local, dtype=jnp.int32)
    live = jnp.repeat(page_picked, PAGE, axis=1) & (positions[None, :] < lengths[:, None])

    key_rows = key_cache.reshape(requests, tok_local, kv_heads, HEAD_DIMENSION)
    scores = (
        jnp.einsum("rkgd,rtkd->rkgt", qgroup, key_rows, preferred_element_type=jnp.float32) * scale
    )
    scores = jnp.where(live[:, None, None, :], scores, NEG)
    peak = jnp.max(scores, axis=-1)
    weights = jnp.where(live[:, None, None, :], jnp.exp(scores - peak[..., None]), 0.0)
    total = jnp.sum(weights, axis=-1)
    values = value_store_cache.reshape(requests, tok_local, kv_heads, HEAD_DIMENSION)
    accum = jnp.einsum(
        "rkgt,rtkd->rkgd", weights.astype(jnp.bfloat16), values, preferred_element_type=jnp.float32
    )
    packed = jnp.concatenate(
        [
            accum.reshape(requests, q_heads, HEAD_DIMENSION),
            peak.reshape(requests, q_heads, 1),
            total.reshape(requests, q_heads, 1),
        ],
        axis=-1,
    )
    packed = jnp.transpose(
        packed.reshape(requests, nseq, heads_dev, HEAD_DIMENSION + 2), (1, 0, 2, 3)
    )
    parts = lax.all_to_all(packed, "seq", 0, 0, tiled=True)
    b_out = parts[..., :HEAD_DIMENSION]
    b_max = parts[..., HEAD_DIMENSION]
    b_sum = parts[..., HEAD_DIMENSION + 1]
    top = jnp.max(b_max, axis=0)
    factor = jnp.exp(b_max - top[None])
    whole_total = jnp.sum(b_sum * factor, axis=0)
    whole_accum = jnp.sum(b_out * factor[..., None], axis=0)
    attended = (
        (whole_accum / whole_total[..., None])
        .reshape(requests, heads_dev * HEAD_DIMENSION)
        .astype(jnp.bfloat16)
    )
    everyone = gather_by_all_to_all(attended, "grp").reshape(-1, attended.shape[1])
    partial = jnp.dot(everyone, w_out, preferred_element_type=jnp.float32)
    partial = partial.reshape(nseq, -1, partial.shape[1])
    pieces = lax.all_to_all(partial, "seq", 0, 0, tiled=True)
    projected = jnp.sum(pieces, axis=0).astype(jnp.bfloat16)
    return (attended, projected)


def solution(mesh):
    return jax.shard_map(
        body,
        mesh=mesh,
        in_specs=(
            P("grp", "seq"),
            P("grp", "seq", None),
            P("grp", "seq", None),
            P("grp", None),
            P("grp"),
            P("seq", "grp"),
        ),
        out_specs=(P("grp", "seq"), P("seq", "grp")),
        check_vma=False,
    )
```

```python
import jax
import jax.numpy as jnp
from jax import lax
from jax.sharding import PartitionSpec as P

HEAD_DIMENSION = 128
PAGE = 64


NEG = -1e30


def gather_by_all_to_all(x, axis):
    n = lax.axis_size(axis)
    return lax.all_to_all(jnp.broadcast_to(x[None], (n,) + x.shape), axis, 0, 0, tiled=True)


def body(query, key_cache, value_store_cache, selected, lengths, w_out):
    nseq = lax.axis_size("seq")
    me = lax.axis_index("seq")
    requests = query.shape[0]
    tok_local = key_cache.shape[1]
    kv_heads = key_cache.shape[2] // HEAD_DIMENSION
    heads_dev = query.shape[1] // HEAD_DIMENSION
    q_heads = heads_dev * nseq
    head_group = q_heads // kv_heads
    scale = HEAD_DIMENSION ** (-0.5)

    heads_all = gather_by_all_to_all(query, "seq")

    pages_local = tok_local // PAGE
    first_page = me * pages_local
    page_ids = first_page + jnp.arange(pages_local, dtype=jnp.int32)
    page_picked = jnp.any(selected[:, :, None] == page_ids[None, None, :], axis=1)
    positions = me * tok_local + jnp.arange(tok_local, dtype=jnp.int32)
    live = jnp.repeat(page_picked, PAGE, axis=1) & (positions[None, :] < lengths[:, None])

    own_kv = (jnp.arange(q_heads) // head_group)[:, None] == jnp.arange(kv_heads)[None, :]
    qfull = jnp.transpose(heads_all, (1, 0, 2)).reshape(requests, q_heads, 1, HEAD_DIMENSION)
    qdiag = jnp.where(own_kv[None, :, :, None], qfull, jnp.zeros((), qfull.dtype)).reshape(
        requests, q_heads, kv_heads * HEAD_DIMENSION
    )
    scores = (
        jnp.einsum("rhc,rtc->rht", qdiag, key_cache, preferred_element_type=jnp.float32) * scale
    )
    scores = jnp.where(live[:, None, :], scores, NEG)
    peak = jnp.max(scores, axis=-1)
    weights = jnp.where(live[:, None, :], jnp.exp(scores - peak[..., None]), 0.0)
    total = jnp.sum(weights, axis=-1)
    full = jnp.einsum(
        "rht,rtc->rhc", weights.astype(jnp.bfloat16), value_store_cache, preferred_element_type=jnp.float32
    ).reshape(requests, q_heads, kv_heads, HEAD_DIMENSION)
    accum = jnp.sum(jnp.where(own_kv[None, :, :, None], full, 0.0), axis=2)
    packed = jnp.concatenate(
        [
            accum.reshape(requests, q_heads, HEAD_DIMENSION),
            peak.reshape(requests, q_heads, 1),
            total.reshape(requests, q_heads, 1),
        ],
        axis=-1,
    )
    packed = jnp.transpose(
        packed.reshape(requests, nseq, heads_dev, HEAD_DIMENSION + 2), (1, 0, 2, 3)
    )
    parts = lax.all_to_all(packed, "seq", 0, 0, tiled=True)
    b_out = parts[..., :HEAD_DIMENSION]
    b_max = parts[..., HEAD_DIMENSION]
    b_sum = parts[..., HEAD_DIMENSION + 1]
    top = jnp.max(b_max, axis=0)
    factor = jnp.exp(b_max - top[None])
    whole_total = jnp.sum(b_sum * factor, axis=0)
    whole_accum = jnp.sum(b_out * factor[..., None], axis=0)
    attended = (
        (whole_accum / whole_total[..., None])
        .reshape(requests, heads_dev * HEAD_DIMENSION)
        .astype(jnp.bfloat16)
    )
    everyone = gather_by_all_to_all(attended, "grp").reshape(-1, attended.shape[1])
    partial = jnp.dot(everyone, w_out, preferred_element_type=jnp.float32)
    partial = partial.reshape(nseq, -1, partial.shape[1])
    pieces = lax.all_to_all(partial, "seq", 0, 0, tiled=True)
    projected = jnp.sum(pieces, axis=0).astype(jnp.bfloat16)
    return (attended, projected)


def solution(mesh):
    return jax.shard_map(
        body,
        mesh=mesh,
        in_specs=(
            P("grp", "seq"),
            P("grp", "seq", None),
            P("grp", "seq", None),
            P("grp", None),
            P("grp"),
            P("seq", "grp"),
        ),
        out_specs=(P("grp", "seq"), P("seq", "grp")),
        check_vma=False,
    )
```

```python
import functools

import jax
import jax.numpy as jnp
from jax import lax
from jax.experimental import pallas as pl
from jax.sharding import PartitionSpec as P

HEAD_DIMENSION = 128
PAGE = 64


NEG = -1e30


def gather_by_all_to_all(x, axis):
    n = lax.axis_size(axis)
    return lax.all_to_all(jnp.broadcast_to(x[None], (n,) + x.shape), axis, 0, 0, tiled=True)


def attention_kernel(q_ref, live_ref, k_ref, v_ref, acc_ref, stat_ref, *, scale, head_group):
    q = q_ref[0]
    live = live_ref[0] > 0
    scores = lax.dot_general(
        q, k_ref[0], (((1,), (1,)), ((), ())), preferred_element_type=jnp.float32
    ) * scale
    scores = jnp.where(live, scores, NEG)
    peak = jnp.max(scores, axis=-1, keepdims=True)
    weights = jnp.where(live, jnp.exp(scores - peak), 0.0)
    total = jnp.sum(weights, axis=-1, keepdims=True)
    full = jnp.dot(weights.astype(jnp.bfloat16), v_ref[0], preferred_element_type=jnp.float32)
    q_heads = q.shape[0]
    for kv in range(q_heads // head_group):
        rows = slice(kv * head_group, (kv + 1) * head_group)
        acc_ref[0, rows, :] = full[rows, kv * HEAD_DIMENSION:(kv + 1) * HEAD_DIMENSION]
    lane = lax.broadcasted_iota(jnp.int32, stat_ref.shape[1:], 1)
    stat_ref[0] = jnp.where(lane == 0, peak, jnp.where(lane == 1, total, 0.0))


def attention(qdiag, live, key_cache, value_store_cache, scale, head_group):
    requests, q_heads, width = qdiag.shape
    tok = key_cache.shape[1]
    kernel = functools.partial(attention_kernel, scale=scale, head_group=head_group)
    flops = 4 * requests * q_heads * tok * width
    nbytes = 2 * (key_cache.size + value_store_cache.size + qdiag.size)
    return pl.pallas_call(
        kernel,
        grid=(requests,),
        in_specs=[
            pl.BlockSpec((1, q_heads, width), lambda r: (r, 0, 0)),
            pl.BlockSpec((1, 1, tok), lambda r: (r, 0, 0)),
            pl.BlockSpec((1, tok, width), lambda r: (r, 0, 0)),
            pl.BlockSpec((1, tok, width), lambda r: (r, 0, 0)),
        ],
        out_specs=[
            pl.BlockSpec((1, q_heads, HEAD_DIMENSION), lambda r: (r, 0, 0)),
            pl.BlockSpec((1, q_heads, HEAD_DIMENSION), lambda r: (r, 0, 0)),
        ],
        out_shape=[
            jax.ShapeDtypeStruct((requests, q_heads, HEAD_DIMENSION), jnp.float32),
            jax.ShapeDtypeStruct((requests, q_heads, HEAD_DIMENSION), jnp.float32),
        ],
        cost_estimate=pl.CostEstimate(
            flops=flops, transcendentals=requests * q_heads * tok, bytes_accessed=nbytes
        ),
    )(qdiag, live.astype(jnp.int32).reshape(requests, 1, tok), key_cache, value_store_cache)


def body(query, key_cache, value_store_cache, selected, lengths, w_out):
    nseq = lax.axis_size("seq")
    me = lax.axis_index("seq")
    requests = query.shape[0]
    tok_local = key_cache.shape[1]
    kv_heads = key_cache.shape[2] // HEAD_DIMENSION
    heads_dev = query.shape[1] // HEAD_DIMENSION
    q_heads = heads_dev * nseq
    head_group = q_heads // kv_heads
    scale = HEAD_DIMENSION ** (-0.5)

    heads_all = gather_by_all_to_all(query, "seq")

    pages_local = tok_local // PAGE
    first_page = me * pages_local
    page_ids = first_page + jnp.arange(pages_local, dtype=jnp.int32)
    page_picked = jnp.any(selected[:, :, None] == page_ids[None, None, :], axis=1)
    positions = me * tok_local + jnp.arange(tok_local, dtype=jnp.int32)
    live = jnp.repeat(page_picked, PAGE, axis=1) & (positions[None, :] < lengths[:, None])

    own_kv = (jnp.arange(q_heads) // head_group)[:, None] == jnp.arange(kv_heads)[None, :]
    qfull = jnp.transpose(heads_all, (1, 0, 2)).reshape(requests, q_heads, 1, HEAD_DIMENSION)
    qdiag = jnp.where(own_kv[None, :, :, None], qfull, jnp.zeros((), qfull.dtype)).reshape(
        requests, q_heads, kv_heads * HEAD_DIMENSION
    )
    accum, stats = attention(qdiag, live, key_cache, value_store_cache, scale, head_group)
    peak = stats[..., 0]
    total = stats[..., 1]
    packed = jnp.concatenate(
        [
            accum.reshape(requests, q_heads, HEAD_DIMENSION),
            peak.reshape(requests, q_heads, 1),
            total.reshape(requests, q_heads, 1),
        ],
        axis=-1,
    )
    packed = jnp.transpose(
        packed.reshape(requests, nseq, heads_dev, HEAD_DIMENSION + 2), (1, 0, 2, 3)
    )
    parts = lax.all_to_all(packed, "seq", 0, 0, tiled=True)
    b_out = parts[..., :HEAD_DIMENSION]
    b_max = parts[..., HEAD_DIMENSION]
    b_sum = parts[..., HEAD_DIMENSION + 1]
    top = jnp.max(b_max, axis=0)
    factor = jnp.exp(b_max - top[None])
    whole_total = jnp.sum(b_sum * factor, axis=0)
    whole_accum = jnp.sum(b_out * factor[..., None], axis=0)
    attended = (
        (whole_accum / whole_total[..., None])
        .reshape(requests, heads_dev * HEAD_DIMENSION)
        .astype(jnp.bfloat16)
    )
    everyone = gather_by_all_to_all(attended, "grp").reshape(-1, attended.shape[1])
    partial = jnp.dot(everyone, w_out, preferred_element_type=jnp.float32)
    partial = partial.reshape(nseq, -1, partial.shape[1])
    pieces = lax.all_to_all(partial, "seq", 0, 0, tiled=True)
    projected = jnp.sum(pieces, axis=0).astype(jnp.bfloat16)
    return (attended, projected)


def solution(mesh):
    return jax.shard_map(
        body,
        mesh=mesh,
        in_specs=(
            P("grp", "seq"),
            P("grp", "seq", None),
            P("grp", "seq", None),
            P("grp", None),
            P("grp"),
            P("seq", "grp"),
        ),
        out_specs=(P("grp", "seq"), P("seq", "grp")),
        check_vma=False,
    )
```

```python
import functools

import jax
import jax.numpy as jnp
from jax import lax
from jax.experimental import pallas as pl
from jax.experimental.pallas import tpu as pltpu
from jax.sharding import PartitionSpec as P

HEAD_DIMENSION = 128
PAGE = 64


NEG = -1e30


def gather_by_all_to_all(x, axis):
    n = lax.axis_size(axis)
    return lax.all_to_all(jnp.broadcast_to(x[None], (n,) + x.shape), axis, 0, 0, tiled=True)


def attention_kernel(
    table_ref, count_ref, limit_ref, q_ref, k_hbm, v_hbm, acc_ref, stat_ref, k_buf, v_buf, sem,
    *, scale, head_group,
):
    requests, q_heads, width = q_ref.shape
    tok = k_buf.shape[1]
    pages = tok // PAGE

    def copy(r, j, which):
        page = table_ref[r, j]
        src = pl.ds(pl.multiple_of(page * PAGE, PAGE), PAGE)
        dst = pl.ds(pl.multiple_of(j * PAGE, PAGE), PAGE)
        hbm, buf = (k_hbm, k_buf) if which == 0 else (v_hbm, v_buf)
        return pltpu.make_async_copy(hbm.at[r, src, :], buf.at[r, dst, :], sem.at[r, which, j])

    for r in range(requests):
        def start(j, carry, r=r):
            copy(r, j, 0).start()
            copy(r, j, 1).start()
            return carry

        lax.fori_loop(0, count_ref[r], start, 0)

    lane = lax.broadcasted_iota(jnp.int32, (1, tok), 1)
    slot = lane // PAGE
    within = lane % PAGE
    stat_lane = lax.broadcasted_iota(jnp.int32, (q_heads, HEAD_DIMENSION), 1)
    for r in range(requests):
        count = count_ref[r]

        def clear(j, carry, r=r):
            v_buf[r, pl.ds(pl.multiple_of(j * PAGE, PAGE), PAGE), :] = jnp.zeros((PAGE, width), v_buf.dtype)
            return carry

        lax.fori_loop(count, pages, clear, 0)

        def wait_keys(j, carry, r=r):
            copy(r, j, 0).wait()
            return carry

        lax.fori_loop(0, count, wait_keys, 0)
        limit = jnp.full((1, tok), -1, jnp.int32)
        for j in range(pages):
            limit = jnp.where(slot == j, limit_ref[r] - table_ref[r, j] * PAGE, limit)
        live = (slot < count) & (within < limit)
        scores = lax.dot_general(
            q_ref[r], k_buf[r], (((1,), (1,)), ((), ())), preferred_element_type=jnp.float32
        ) * scale
        scores = jnp.where(live, scores, NEG)
        peak = jnp.max(scores, axis=-1, keepdims=True)
        weights = jnp.where(live, jnp.exp(scores - peak), 0.0)
        total = jnp.sum(weights, axis=-1, keepdims=True)

        def wait_values(j, carry, r=r):
            copy(r, j, 1).wait()
            return carry

        lax.fori_loop(0, count, wait_values, 0)
        full = jnp.dot(weights.astype(jnp.bfloat16), v_buf[r], preferred_element_type=jnp.float32)
        for kv in range(q_heads // head_group):
            rows = slice(kv * head_group, (kv + 1) * head_group)
            acc_ref[r, rows, :] = full[rows, kv * HEAD_DIMENSION:(kv + 1) * HEAD_DIMENSION]
        stat_ref[r] = jnp.where(stat_lane == 0, peak, jnp.where(stat_lane == 1, total, 0.0))


def attention(qdiag, table, count, limit, key_cache, value_store_cache, scale, head_group):
    requests, q_heads, width = qdiag.shape
    tok = key_cache.shape[1]
    kernel = functools.partial(attention_kernel, scale=scale, head_group=head_group)
    flops = 4 * requests * q_heads * tok * width
    nbytes = 2 * (key_cache.size + value_store_cache.size + qdiag.size)
    smem = pl.BlockSpec(memory_space=pltpu.SMEM)
    vmem = pl.BlockSpec(memory_space=pltpu.VMEM)
    hbm = pl.BlockSpec(memory_space=pl.ANY)
    return pl.pallas_call(
        kernel,
        in_specs=[smem, smem, smem, vmem, hbm, hbm],
        out_specs=[vmem, vmem],
        out_shape=[
            jax.ShapeDtypeStruct((requests, q_heads, HEAD_DIMENSION), jnp.float32),
            jax.ShapeDtypeStruct((requests, q_heads, HEAD_DIMENSION), jnp.float32),
        ],
        scratch_shapes=[
            pltpu.VMEM((requests, tok, width), key_cache.dtype),
            pltpu.VMEM((requests, tok, width), value_store_cache.dtype),
            pltpu.SemaphoreType.DMA((requests, 2, tok // PAGE)),
        ],
        compiler_params=pltpu.CompilerParams(vmem_limit_bytes=48 * 1024 * 1024),
        cost_estimate=pl.CostEstimate(
            flops=flops, transcendentals=requests * q_heads * tok, bytes_accessed=nbytes
        ),
    )(table, count, limit, qdiag, key_cache, value_store_cache)


def body(query, key_cache, value_store_cache, selected, lengths, w_out):
    nseq = lax.axis_size("seq")
    me = lax.axis_index("seq")
    requests = query.shape[0]
    tok_local = key_cache.shape[1]
    kv_heads = key_cache.shape[2] // HEAD_DIMENSION
    heads_dev = query.shape[1] // HEAD_DIMENSION
    q_heads = heads_dev * nseq
    head_group = q_heads // kv_heads
    scale = HEAD_DIMENSION ** (-0.5)

    heads_all = gather_by_all_to_all(query, "seq")

    pages_local = tok_local // PAGE
    page_ids = me * pages_local + jnp.arange(pages_local, dtype=jnp.int32)
    page_picked = jnp.any(selected[:, :, None] == page_ids[None, None, :], axis=1)
    count = jnp.sum(page_picked.astype(jnp.int32), axis=1)
    local = jnp.arange(pages_local, dtype=jnp.int32)
    rank = jnp.sum(
        (page_picked[:, None, :] & (local[None, None, :] <= local[None, :, None])).astype(jnp.int32), axis=2
    ) - 1
    table = jnp.sum(
        jnp.where(page_picked[:, None, :] & (rank[:, None, :] == local[None, :, None]), local[None, None, :], 0),
        axis=2,
    ).astype(jnp.int32)
    limit = (lengths - me * tok_local).astype(jnp.int32)

    own_kv = (jnp.arange(q_heads) // head_group)[:, None] == jnp.arange(kv_heads)[None, :]
    qfull = jnp.transpose(heads_all, (1, 0, 2)).reshape(requests, q_heads, 1, HEAD_DIMENSION)
    qdiag = jnp.where(own_kv[None, :, :, None], qfull, jnp.zeros((), qfull.dtype)).reshape(
        requests, q_heads, kv_heads * HEAD_DIMENSION
    )
    accum, stats = attention(qdiag, table, count, limit, key_cache, value_store_cache, scale, head_group)
    peak = stats[..., 0]
    total = stats[..., 1]
    packed = jnp.concatenate(
        [
            accum.reshape(requests, q_heads, HEAD_DIMENSION),
            peak.reshape(requests, q_heads, 1),
            total.reshape(requests, q_heads, 1),
        ],
        axis=-1,
    )
    packed = jnp.transpose(
        packed.reshape(requests, nseq, heads_dev, HEAD_DIMENSION + 2), (1, 0, 2, 3)
    )
    parts = lax.all_to_all(packed, "seq", 0, 0, tiled=True)
    b_out = parts[..., :HEAD_DIMENSION]
    b_max = parts[..., HEAD_DIMENSION]
    b_sum = parts[..., HEAD_DIMENSION + 1]
    top = jnp.max(b_max, axis=0)
    factor = jnp.exp(b_max - top[None])
    whole_total = jnp.sum(b_sum * factor, axis=0)
    whole_accum = jnp.sum(b_out * factor[..., None], axis=0)
    attended = (
        (whole_accum / whole_total[..., None])
        .reshape(requests, heads_dev * HEAD_DIMENSION)
        .astype(jnp.bfloat16)
    )
    everyone = gather_by_all_to_all(attended, "grp").reshape(-1, attended.shape[1])
    partial = jnp.dot(everyone, w_out, preferred_element_type=jnp.float32)
    partial = partial.reshape(nseq, -1, partial.shape[1])
    pieces = lax.all_to_all(partial, "seq", 0, 0, tiled=True)
    projected = jnp.sum(pieces, axis=0).astype(jnp.bfloat16)
    return (attended, projected)


def solution(mesh):
    return jax.shard_map(
        body,
        mesh=mesh,
        in_specs=(
            P("grp", "seq"),
            P("grp", "seq", None),
            P("grp", "seq", None),
            P("grp", None),
            P("grp"),
            P("seq", "grp"),
        ),
        out_specs=(P("grp", "seq"), P("seq", "grp")),
        check_vma=False,
    )
```

```python
import functools

import jax
import jax.numpy as jnp
from jax import lax
from jax.experimental import pallas as pl
from jax.experimental.pallas import tpu as pltpu
from jax.sharding import PartitionSpec as P

HEAD_DIMENSION = 128
PAGE = 64


NEG = -1e30


def gather_by_all_to_all(x, axis):
    n = lax.axis_size(axis)
    return lax.all_to_all(jnp.broadcast_to(x[None], (n,) + x.shape), axis, 0, 0, tiled=True)


def attention_kernel(h_ref, live_ref, k_ref, v_ref, out_ref, qd_ref, *, scale, head_group):
    _, nseq, local_width = h_ref.shape
    heads_dev = local_width // HEAD_DIMENSION
    q_heads = nseq * heads_dev
    qd_ref[...] = jnp.zeros(qd_ref.shape, qd_ref.dtype)
    for src in range(nseq):
        for i in range(heads_dev):
            h = src * heads_dev + i
            kv = h // head_group
            qd_ref[h:h + 1, kv * HEAD_DIMENSION:(kv + 1) * HEAD_DIMENSION] = h_ref[
                0, src:src + 1, i * HEAD_DIMENSION:(i + 1) * HEAD_DIMENSION
            ].astype(qd_ref.dtype)
    q = qd_ref[...].astype(jnp.bfloat16)
    live = live_ref[0] > 0
    scores = lax.dot_general(
        q, k_ref[0], (((1,), (1,)), ((), ())), preferred_element_type=jnp.float32
    ) * scale
    scores = jnp.where(live, scores, NEG)
    peak = jnp.max(scores, axis=-1, keepdims=True)
    weights = jnp.where(live, jnp.exp(scores - peak), 0.0)
    total = jnp.sum(weights, axis=-1, keepdims=True)
    full = jnp.dot(weights.astype(jnp.bfloat16), v_ref[0], preferred_element_type=jnp.float32)
    lane = lax.broadcasted_iota(jnp.int32, (q_heads, HEAD_DIMENSION), 1)
    stat = jnp.where(lane == 0, peak, jnp.where(lane == 1, total, 0.0))
    for d in range(nseq):
        rows = slice(d * heads_dev, (d + 1) * heads_dev)
        kv = d * heads_dev // head_group
        out_ref[d, 0, :, 0:HEAD_DIMENSION] = full[rows, kv * HEAD_DIMENSION:(kv + 1) * HEAD_DIMENSION]
        out_ref[d, 0, :, HEAD_DIMENSION:] = stat[rows, :]


def attention(heads_all, live, key_cache, value_store_cache, scale, head_group):
    nseq, requests, local_width = heads_all.shape
    heads_dev = local_width // HEAD_DIMENSION
    q_heads = nseq * heads_dev
    tok, width = key_cache.shape[1:]
    kernel = functools.partial(attention_kernel, scale=scale, head_group=head_group)
    flops = 4 * requests * q_heads * tok * width
    nbytes = 2 * (key_cache.size + value_store_cache.size + heads_all.size)
    return pl.pallas_call(
        kernel,
        grid=(requests,),
        in_specs=[
            pl.BlockSpec((1, nseq, local_width), lambda r: (r, 0, 0)),
            pl.BlockSpec((1, 1, tok), lambda r: (r, 0, 0)),
            pl.BlockSpec((1, tok, width), lambda r: (r, 0, 0)),
            pl.BlockSpec((1, tok, width), lambda r: (r, 0, 0)),
        ],
        out_specs=pl.BlockSpec((nseq, 1, heads_dev, 2 * HEAD_DIMENSION), lambda r: (0, r, 0, 0)),
        out_shape=jax.ShapeDtypeStruct((nseq, requests, heads_dev, 2 * HEAD_DIMENSION), jnp.float32),
        scratch_shapes=[pltpu.VMEM((q_heads, width), jnp.float32)],
        cost_estimate=pl.CostEstimate(
            flops=flops, transcendentals=requests * q_heads * tok, bytes_accessed=nbytes
        ),
    )(jnp.transpose(heads_all, (1, 0, 2)), live.astype(jnp.int32).reshape(requests, 1, tok), key_cache, value_store_cache)


def body(query, key_cache, value_store_cache, selected, lengths, w_out):
    nseq = lax.axis_size("seq")
    me = lax.axis_index("seq")
    requests = query.shape[0]
    tok_local = key_cache.shape[1]
    kv_heads = key_cache.shape[2] // HEAD_DIMENSION
    heads_dev = query.shape[1] // HEAD_DIMENSION
    q_heads = heads_dev * nseq
    head_group = q_heads // kv_heads
    scale = HEAD_DIMENSION ** (-0.5)

    heads_all = gather_by_all_to_all(query, "seq")

    pages_local = tok_local // PAGE
    first_page = me * pages_local
    page_ids = first_page + jnp.arange(pages_local, dtype=jnp.int32)
    page_picked = jnp.any(selected[:, :, None] == page_ids[None, None, :], axis=1)
    positions = me * tok_local + jnp.arange(tok_local, dtype=jnp.int32)
    live = jnp.repeat(page_picked, PAGE, axis=1) & (positions[None, :] < lengths[:, None])

    packed = attention(heads_all, live, key_cache, value_store_cache, scale, head_group)
    parts = lax.all_to_all(packed, "seq", 0, 0, tiled=True)
    b_out = parts[..., :HEAD_DIMENSION]
    b_max = parts[..., HEAD_DIMENSION]
    b_sum = parts[..., HEAD_DIMENSION + 1]
    top = jnp.max(b_max, axis=0)
    factor = jnp.exp(b_max - top[None])
    whole_total = jnp.sum(b_sum * factor, axis=0)
    whole_accum = jnp.sum(b_out * factor[..., None], axis=0)
    attended = (
        (whole_accum / whole_total[..., None])
        .reshape(requests, heads_dev * HEAD_DIMENSION)
        .astype(jnp.bfloat16)
    )
    everyone = gather_by_all_to_all(attended, "grp").reshape(-1, attended.shape[1])
    partial = jnp.dot(everyone, w_out, preferred_element_type=jnp.float32)
    partial = partial.reshape(nseq, -1, partial.shape[1])
    pieces = lax.all_to_all(partial, "seq", 0, 0, tiled=True)
    projected = jnp.sum(pieces, axis=0).astype(jnp.bfloat16)
    return (attended, projected)


def solution(mesh):
    return jax.shard_map(
        body,
        mesh=mesh,
        in_specs=(
            P("grp", "seq"),
            P("grp", "seq", None),
            P("grp", "seq", None),
            P("grp", None),
            P("grp"),
            P("seq", "grp"),
        ),
        out_specs=(P("grp", "seq"), P("seq", "grp")),
        check_vma=False,
    )
```

```python
import functools

import jax
import jax.numpy as jnp
from jax import lax
from jax.experimental import pallas as pl
from jax.experimental.pallas import tpu as pltpu
from jax.sharding import PartitionSpec as P

HEAD_DIMENSION = 128
PAGE = 64


NEG = -1e30


def gather_by_all_to_all(x, axis):
    n = lax.axis_size(axis)
    return lax.all_to_all(jnp.broadcast_to(x[None], (n,) + x.shape), axis, 0, 0, tiled=True)


def attention_kernel(h_ref, live_ref, k_ref, v_ref, out_ref, qd_ref, *, scale, head_group):
    nseq, requests, local_width = h_ref.shape
    heads_dev = local_width // HEAD_DIMENSION
    q_heads = nseq * heads_dev

    @pl.when(pl.program_id(0) == 0)
    def _():
        qd_ref[...] = jnp.zeros(qd_ref.shape, qd_ref.dtype)
        for r in range(requests):
            for src in range(nseq):
                for i in range(heads_dev):
                    h = src * heads_dev + i
                    kv = h // head_group
                    qd_ref[r, h:h + 1, kv * HEAD_DIMENSION:(kv + 1) * HEAD_DIMENSION] = h_ref[
                        src, r:r + 1, i * HEAD_DIMENSION:(i + 1) * HEAD_DIMENSION
                    ].astype(qd_ref.dtype)

    q = qd_ref[pl.program_id(0)].astype(jnp.bfloat16)
    live = live_ref[0] > 0
    scores = lax.dot_general(
        q, k_ref[0], (((1,), (1,)), ((), ())), preferred_element_type=jnp.float32
    ) * scale
    scores = jnp.where(live, scores, NEG)
    peak = jnp.max(scores, axis=-1, keepdims=True)
    weights = jnp.where(live, jnp.exp(scores - peak), 0.0)
    total = jnp.sum(weights, axis=-1, keepdims=True)
    full = jnp.dot(weights.astype(jnp.bfloat16), v_ref[0], preferred_element_type=jnp.float32)
    lane = lax.broadcasted_iota(jnp.int32, (q_heads, HEAD_DIMENSION), 1)
    stat = jnp.where(lane == 0, peak, jnp.where(lane == 1, total, 0.0))
    for d in range(nseq):
        rows = slice(d * heads_dev, (d + 1) * heads_dev)
        kv = d * heads_dev // head_group
        out_ref[d, 0, :, 0:HEAD_DIMENSION] = full[rows, kv * HEAD_DIMENSION:(kv + 1) * HEAD_DIMENSION]
        out_ref[d, 0, :, HEAD_DIMENSION:] = stat[rows, :]


def attention(heads_all, live, key_cache, value_store_cache, scale, head_group):
    nseq, requests, local_width = heads_all.shape
    heads_dev = local_width // HEAD_DIMENSION
    q_heads = nseq * heads_dev
    tok, width = key_cache.shape[1:]
    kernel = functools.partial(attention_kernel, scale=scale, head_group=head_group)
    flops = 4 * requests * q_heads * tok * width
    nbytes = 2 * (key_cache.size + value_store_cache.size + heads_all.size)
    return pl.pallas_call(
        kernel,
        grid=(requests,),
        in_specs=[
            pl.BlockSpec((nseq, requests, local_width), lambda r: (0, 0, 0)),
            pl.BlockSpec((1, 1, tok), lambda r: (r, 0, 0)),
            pl.BlockSpec((1, tok, width), lambda r: (r, 0, 0)),
            pl.BlockSpec((1, tok, width), lambda r: (r, 0, 0)),
        ],
        out_specs=pl.BlockSpec((nseq, 1, heads_dev, 2 * HEAD_DIMENSION), lambda r: (0, r, 0, 0)),
        out_shape=jax.ShapeDtypeStruct((nseq, requests, heads_dev, 2 * HEAD_DIMENSION), jnp.float32),
        scratch_shapes=[pltpu.VMEM((requests, q_heads, width), jnp.float32)],
        cost_estimate=pl.CostEstimate(
            flops=flops, transcendentals=requests * q_heads * tok, bytes_accessed=nbytes
        ),
    )(heads_all, live.astype(jnp.int32).reshape(requests, 1, tok), key_cache, value_store_cache)


def combine_kernel(p_ref, att_ref, bcast_ref):
    nseq, requests, heads_dev, _ = p_ref.shape
    rows = []
    for r in range(requests):
        part = p_ref[:, r]
        b_out = part[:, :, :HEAD_DIMENSION]
        b_max = part[:, :, HEAD_DIMENSION:HEAD_DIMENSION + 1]
        b_sum = part[:, :, HEAD_DIMENSION + 1:HEAD_DIMENSION + 2]
        top = jnp.max(b_max, axis=0)
        factor = jnp.exp(b_max - top[None])
        whole_total = jnp.sum(b_sum * factor, axis=0)
        whole_accum = jnp.sum(b_out * factor, axis=0)
        merged = whole_accum / whole_total
        rows.append(jnp.concatenate([merged[i:i + 1] for i in range(heads_dev)], axis=1))
    attended = jnp.concatenate(rows, axis=0).astype(att_ref.dtype)
    att_ref[...] = attended
    bcast_ref[...] = jnp.broadcast_to(attended[None], bcast_ref.shape)


def combine(parts, bcast_count):
    nseq, requests, heads_dev, _ = parts.shape
    vmem = pl.BlockSpec(memory_space=pltpu.VMEM)
    width = heads_dev * HEAD_DIMENSION
    return pl.pallas_call(
        combine_kernel,
        in_specs=[vmem],
        out_specs=[vmem, vmem],
        out_shape=[
            jax.ShapeDtypeStruct((requests, width), jnp.bfloat16),
            jax.ShapeDtypeStruct((bcast_count, requests, width), jnp.bfloat16),
        ],
    )(parts)


def body(query, key_cache, value_store_cache, selected, lengths, w_out):
    nseq = lax.axis_size("seq")
    me = lax.axis_index("seq")
    requests = query.shape[0]
    tok_local = key_cache.shape[1]
    kv_heads = key_cache.shape[2] // HEAD_DIMENSION
    heads_dev = query.shape[1] // HEAD_DIMENSION
    q_heads = heads_dev * nseq
    head_group = q_heads // kv_heads
    scale = HEAD_DIMENSION ** (-0.5)

    heads_all = gather_by_all_to_all(query, "seq")

    pages_local = tok_local // PAGE
    first_page = me * pages_local
    page_ids = first_page + jnp.arange(pages_local, dtype=jnp.int32)
    page_picked = jnp.any(selected[:, :, None] == page_ids[None, None, :], axis=1)
    positions = me * tok_local + jnp.arange(tok_local, dtype=jnp.int32)
    live = jnp.repeat(page_picked, PAGE, axis=1) & (positions[None, :] < lengths[:, None])

    packed = attention(heads_all, live, key_cache, value_store_cache, scale, head_group)
    parts = lax.all_to_all(packed, "seq", 0, 0, tiled=True)
    attended, spread = combine(parts, lax.axis_size("grp"))
    everyone = lax.all_to_all(spread, "grp", 0, 0, tiled=True).reshape(-1, attended.shape[1])
    partial = jnp.dot(everyone, w_out, preferred_element_type=jnp.float32)
    partial = partial.reshape(nseq, -1, partial.shape[1])
    pieces = lax.all_to_all(partial, "seq", 0, 0, tiled=True)
    projected = jnp.sum(pieces, axis=0).astype(jnp.bfloat16)
    return (attended, projected)


def solution(mesh):
    return jax.shard_map(
        body,
        mesh=mesh,
        in_specs=(
            P("grp", "seq"),
            P("grp", "seq", None),
            P("grp", "seq", None),
            P("grp", None),
            P("grp"),
            P("seq", "grp"),
        ),
        out_specs=(P("grp", "seq"), P("seq", "grp")),
        check_vma=False,
    )
```

```python
import functools

import jax
import jax.numpy as jnp
from jax import lax
from jax.experimental import pallas as pl
from jax.experimental.pallas import tpu as pltpu
from jax.sharding import PartitionSpec as P

HEAD_DIMENSION = 128
PAGE = 64


NEG = -1e30


def gather_by_all_to_all(x, axis):
    n = lax.axis_size(axis)
    return lax.all_to_all(jnp.broadcast_to(x[None], (n,) + x.shape), axis, 0, 0, tiled=True)


def attention_kernel(sel_ref, lim_ref, base_ref, h_ref, k_ref, v_ref, out_ref, qd_ref, *, scale, head_group):
    _, nseq, local_width = h_ref.shape
    heads_dev = local_width // HEAD_DIMENSION
    q_heads = nseq * heads_dev
    qd_ref[...] = jnp.zeros(qd_ref.shape, qd_ref.dtype)
    for src in range(nseq):
        for i in range(heads_dev):
            h = src * heads_dev + i
            kv = h // head_group
            qd_ref[h:h + 1, kv * HEAD_DIMENSION:(kv + 1) * HEAD_DIMENSION] = h_ref[
                0, src:src + 1, i * HEAD_DIMENSION:(i + 1) * HEAD_DIMENSION
            ].astype(qd_ref.dtype)
    q = qd_ref[...].astype(jnp.bfloat16)
    r = pl.program_id(0)
    tok = k_ref.shape[1]
    lane = lax.broadcasted_iota(jnp.int32, (1, tok), 1)
    page = base_ref[0] + lane // PAGE
    picked = page == sel_ref[r, 0]
    for j in range(1, sel_ref.shape[1]):
        picked = picked | (page == sel_ref[r, j])
    live = picked & (lane < lim_ref[r])
    scores = lax.dot_general(
        q, k_ref[0], (((1,), (1,)), ((), ())), preferred_element_type=jnp.float32
    ) * scale
    scores = jnp.where(live, scores, NEG)
    peak = jnp.max(scores, axis=-1, keepdims=True)
    weights = jnp.where(live, jnp.exp(scores - peak), 0.0)
    total = jnp.sum(weights, axis=-1, keepdims=True)
    full = jnp.dot(weights.astype(jnp.bfloat16), v_ref[0], preferred_element_type=jnp.float32)
    lane = lax.broadcasted_iota(jnp.int32, (q_heads, HEAD_DIMENSION), 1)
    stat = jnp.where(lane == 0, peak, jnp.where(lane == 1, total, 0.0))
    for d in range(nseq):
        rows = slice(d * heads_dev, (d + 1) * heads_dev)
        kv = d * heads_dev // head_group
        out_ref[d, 0, :, 0:HEAD_DIMENSION] = full[rows, kv * HEAD_DIMENSION:(kv + 1) * HEAD_DIMENSION]
        out_ref[d, 0, :, HEAD_DIMENSION:] = stat[rows, :]


def attention(heads_all, selected, limit, base, key_cache, value_store_cache, scale, head_group):
    nseq, requests, local_width = heads_all.shape
    heads_dev = local_width // HEAD_DIMENSION
    q_heads = nseq * heads_dev
    tok, width = key_cache.shape[1:]
    kernel = functools.partial(attention_kernel, scale=scale, head_group=head_group)
    flops = 4 * requests * q_heads * tok * width
    nbytes = 2 * (key_cache.size + value_store_cache.size + heads_all.size)
    return pl.pallas_call(
        kernel,
        grid=(requests,),
        in_specs=[
            pl.BlockSpec(memory_space=pltpu.SMEM),
            pl.BlockSpec(memory_space=pltpu.SMEM),
            pl.BlockSpec(memory_space=pltpu.SMEM),
            pl.BlockSpec((1, nseq, local_width), lambda r: (r, 0, 0)),
            pl.BlockSpec((1, tok, width), lambda r: (r, 0, 0)),
            pl.BlockSpec((1, tok, width), lambda r: (r, 0, 0)),
        ],
        out_specs=pl.BlockSpec((nseq, 1, heads_dev, 2 * HEAD_DIMENSION), lambda r: (0, r, 0, 0)),
        out_shape=jax.ShapeDtypeStruct((nseq, requests, heads_dev, 2 * HEAD_DIMENSION), jnp.float32),
        scratch_shapes=[pltpu.VMEM((q_heads, width), jnp.float32)],
        cost_estimate=pl.CostEstimate(
            flops=flops, transcendentals=requests * q_heads * tok, bytes_accessed=nbytes
        ),
    )(selected, limit, base, jnp.transpose(heads_all, (1, 0, 2)), key_cache, value_store_cache)


def body(query, key_cache, value_store_cache, selected, lengths, w_out):
    nseq = lax.axis_size("seq")
    me = lax.axis_index("seq")
    requests = query.shape[0]
    tok_local = key_cache.shape[1]
    kv_heads = key_cache.shape[2] // HEAD_DIMENSION
    heads_dev = query.shape[1] // HEAD_DIMENSION
    q_heads = heads_dev * nseq
    head_group = q_heads // kv_heads
    scale = HEAD_DIMENSION ** (-0.5)

    heads_all = gather_by_all_to_all(query, "seq")

    limit = (lengths - me * tok_local).astype(jnp.int32)
    base = jnp.reshape(me * (tok_local // PAGE), (1,)).astype(jnp.int32)
    packed = attention(heads_all, selected, limit, base, key_cache, value_store_cache, scale, head_group)
    parts = lax.all_to_all(packed, "seq", 0, 0, tiled=True)
    b_out = parts[..., :HEAD_DIMENSION]
    b_max = parts[..., HEAD_DIMENSION]
    b_sum = parts[..., HEAD_DIMENSION + 1]
    top = jnp.max(b_max, axis=0)
    factor = jnp.exp(b_max - top[None])
    whole_total = jnp.sum(b_sum * factor, axis=0)
    whole_accum = jnp.sum(b_out * factor[..., None], axis=0)
    attended = (
        (whole_accum / whole_total[..., None])
        .reshape(requests, heads_dev * HEAD_DIMENSION)
        .astype(jnp.bfloat16)
    )
    everyone = gather_by_all_to_all(attended, "grp").reshape(-1, attended.shape[1])
    partial = jnp.dot(everyone, w_out, preferred_element_type=jnp.float32)
    partial = partial.reshape(nseq, -1, partial.shape[1])
    pieces = lax.all_to_all(partial, "seq", 0, 0, tiled=True)
    projected = jnp.sum(pieces, axis=0).astype(jnp.bfloat16)
    return (attended, projected)


def solution(mesh):
    return jax.shard_map(
        body,
        mesh=mesh,
        in_specs=(
            P("grp", "seq"),
            P("grp", "seq", None),
            P("grp", "seq", None),
            P("grp", None),
            P("grp"),
            P("seq", "grp"),
        ),
        out_specs=(P("grp", "seq"), P("seq", "grp")),
        check_vma=False,
    )
```

```python
import functools

import jax
import jax.numpy as jnp
from jax import lax
from jax.experimental import pallas as pl
from jax.experimental.pallas import tpu as pltpu
from jax.sharding import PartitionSpec as P

HEAD_DIMENSION = 128
PAGE = 64


NEG = -1e30


def gather_by_all_to_all(x, axis):
    n = lax.axis_size(axis)
    return lax.all_to_all(jnp.broadcast_to(x[None], (n,) + x.shape), axis, 0, 0, tiled=True)


def attention_kernel(sel_ref, lim_ref, base_ref, h_ref, k_ref, v_ref, out_ref, qd_ref, *, scale, head_group):
    _, nseq, local_width = h_ref.shape
    heads_dev = local_width // HEAD_DIMENSION
    q_heads = nseq * heads_dev
    qd_ref[...] = jnp.zeros(qd_ref.shape, qd_ref.dtype)
    for src in range(nseq):
        for i in range(heads_dev):
            h = src * heads_dev + i
            kv = h // head_group
            qd_ref[h:h + 1, kv * HEAD_DIMENSION:(kv + 1) * HEAD_DIMENSION] = h_ref[
                0, src:src + 1, i * HEAD_DIMENSION:(i + 1) * HEAD_DIMENSION
            ].astype(qd_ref.dtype)
    q = qd_ref[...].astype(jnp.bfloat16)
    r = pl.program_id(0)
    tok = k_ref.shape[1]
    lane = lax.broadcasted_iota(jnp.int32, (1, tok), 1)
    page = base_ref[0] + lane // PAGE
    picked = page == sel_ref[r, 0]
    for j in range(1, sel_ref.shape[1]):
        picked = picked | (page == sel_ref[r, j])
    live = picked & (lane < lim_ref[r])
    scores = lax.dot_general(
        q, k_ref[0], (((1,), (1,)), ((), ())), preferred_element_type=jnp.float32
    ) * scale
    scores = jnp.where(live, scores, NEG)
    peak = jnp.max(scores, axis=-1, keepdims=True)
    weights = jnp.where(live, jnp.exp(scores - peak), 0.0)
    total = jnp.sum(weights, axis=-1, keepdims=True)
    full = jnp.dot(weights.astype(jnp.bfloat16), v_ref[0], preferred_element_type=jnp.float32)
    peak_lanes = jnp.broadcast_to(peak, (q_heads, HEAD_DIMENSION))
    total_lanes = jnp.broadcast_to(total, (q_heads, HEAD_DIMENSION))
    for d in range(nseq):
        rows = slice(d * heads_dev, (d + 1) * heads_dev)
        kv = d * heads_dev // head_group
        out_ref[d, 0, :, 0:HEAD_DIMENSION] = full[rows, kv * HEAD_DIMENSION:(kv + 1) * HEAD_DIMENSION]
        out_ref[d, 0, :, HEAD_DIMENSION:2 * HEAD_DIMENSION] = peak_lanes[rows, :]
        out_ref[d, 0, :, 2 * HEAD_DIMENSION:] = total_lanes[rows, :]


def attention(heads_all, selected, limit, base, key_cache, value_store_cache, scale, head_group):
    requests, nseq, local_width = heads_all.shape
    heads_dev = local_width // HEAD_DIMENSION
    q_heads = nseq * heads_dev
    tok, width = key_cache.shape[1:]
    kernel = functools.partial(attention_kernel, scale=scale, head_group=head_group)
    flops = 4 * requests * q_heads * tok * width
    nbytes = 2 * (key_cache.size + value_store_cache.size + heads_all.size)
    return pl.pallas_call(
        kernel,
        grid=(requests,),
        in_specs=[
            pl.BlockSpec(memory_space=pltpu.SMEM),
            pl.BlockSpec(memory_space=pltpu.SMEM),
            pl.BlockSpec(memory_space=pltpu.SMEM),
            pl.BlockSpec((1, nseq, local_width), lambda r: (r, 0, 0)),
            pl.BlockSpec((1, tok, width), lambda r: (r, 0, 0)),
            pl.BlockSpec((1, tok, width), lambda r: (r, 0, 0)),
        ],
        out_specs=pl.BlockSpec((nseq, 1, heads_dev, 3 * HEAD_DIMENSION), lambda r: (0, r, 0, 0)),
        out_shape=jax.ShapeDtypeStruct((nseq, requests, heads_dev, 3 * HEAD_DIMENSION), jnp.float32),
        scratch_shapes=[pltpu.VMEM((q_heads, width), jnp.float32)],
        cost_estimate=pl.CostEstimate(
            flops=flops, transcendentals=requests * q_heads * tok, bytes_accessed=nbytes
        ),
    )(selected, limit, base, heads_all, key_cache, value_store_cache)


def body(query, key_cache, value_store_cache, selected, lengths, w_out):
    nseq = lax.axis_size("seq")
    me = lax.axis_index("seq")
    requests = query.shape[0]
    tok_local = key_cache.shape[1]
    kv_heads = key_cache.shape[2] // HEAD_DIMENSION
    heads_dev = query.shape[1] // HEAD_DIMENSION
    q_heads = heads_dev * nseq
    head_group = q_heads // kv_heads
    scale = HEAD_DIMENSION ** (-0.5)

    heads_all = lax.all_to_all(
        jnp.broadcast_to(query[:, None, :], (requests, nseq, query.shape[1])), "seq", 1, 1, tiled=True
    )

    limit = (lengths - me * tok_local).astype(jnp.int32)
    base = jnp.reshape(me * (tok_local // PAGE), (1,)).astype(jnp.int32)
    packed = attention(heads_all, selected, limit, base, key_cache, value_store_cache, scale, head_group)
    parts = lax.all_to_all(packed, "seq", 0, 0, tiled=True)
    b_out = parts[..., :HEAD_DIMENSION]
    b_max = parts[..., HEAD_DIMENSION:2 * HEAD_DIMENSION]
    b_sum = parts[..., 2 * HEAD_DIMENSION:]
    top = jnp.max(b_max, axis=0)
    factor = jnp.exp(b_max - top[None])
    whole_total = jnp.sum(b_sum * factor, axis=0)
    whole_accum = jnp.sum(b_out * factor, axis=0)
    attended = (
        (whole_accum / whole_total)
        .reshape(requests, heads_dev * HEAD_DIMENSION)
        .astype(jnp.bfloat16)
    )
    everyone = gather_by_all_to_all(attended, "grp").reshape(-1, attended.shape[1])
    partial = jnp.dot(everyone, w_out, preferred_element_type=jnp.float32)
    partial = partial.reshape(nseq, -1, partial.shape[1])
    pieces = lax.all_to_all(partial, "seq", 0, 0, tiled=True)
    projected = jnp.sum(pieces, axis=0).astype(jnp.bfloat16)
    return (attended, projected)


def solution(mesh):
    return jax.shard_map(
        body,
        mesh=mesh,
        in_specs=(
            P("grp", "seq"),
            P("grp", "seq", None),
            P("grp", "seq", None),
            P("grp", None),
            P("grp"),
            P("seq", "grp"),
        ),
        out_specs=(P("grp", "seq"), P("seq", "grp")),
        check_vma=False,
    )
```

```python
import functools

import jax
import jax.numpy as jnp
from jax import lax
from jax.experimental import pallas as pl
from jax.experimental.pallas import tpu as pltpu
from jax.sharding import PartitionSpec as P

HEAD_DIMENSION = 128
PAGE = 64


NEG = -1e30


def gather_by_all_to_all(x, axis):
    n = lax.axis_size(axis)
    return lax.all_to_all(jnp.broadcast_to(x[None], (n,) + x.shape), axis, 0, 0, tiled=True)


def attention_kernel(sel_ref, lim_ref, base_ref, h_ref, k_ref, v_ref, out_ref, qd_ref, *, scale, head_group):
    _, nseq, local_width = h_ref.shape
    heads_dev = local_width // HEAD_DIMENSION
    q_heads = nseq * heads_dev
    qd_ref[...] = jnp.zeros(qd_ref.shape, qd_ref.dtype)
    for src in range(nseq):
        for i in range(heads_dev):
            h = src * heads_dev + i
            kv = h // head_group
            qd_ref[h:h + 1, kv * HEAD_DIMENSION:(kv + 1) * HEAD_DIMENSION] = h_ref[
                0, src:src + 1, i * HEAD_DIMENSION:(i + 1) * HEAD_DIMENSION
            ].astype(qd_ref.dtype)
    q = qd_ref[...].astype(jnp.bfloat16)
    r = pl.program_id(0)
    tok = k_ref.shape[1]
    lane = lax.broadcasted_iota(jnp.int32, (1, tok), 1)
    page = base_ref[0] + lane // PAGE
    picked = page == sel_ref[r, 0]
    for j in range(1, sel_ref.shape[1]):
        picked = picked | (page == sel_ref[r, j])
    live = picked & (lane < lim_ref[r])
    scores = lax.dot_general(
        q, k_ref[0], (((1,), (1,)), ((), ())), preferred_element_type=jnp.float32
    ) * scale
    scores = jnp.where(live, scores, NEG)
    peak = jnp.max(scores, axis=-1, keepdims=True)
    weights = jnp.where(live, jnp.exp(scores - peak), 0.0)
    total = jnp.sum(weights, axis=-1, keepdims=True)
    full = jnp.dot(weights.astype(jnp.bfloat16), v_ref[0], preferred_element_type=jnp.float32)
    peak_lanes = jnp.broadcast_to(peak, (q_heads, HEAD_DIMENSION))
    total_lanes = jnp.broadcast_to(total, (q_heads, HEAD_DIMENSION))
    for d in range(nseq):
        rows = slice(d * heads_dev, (d + 1) * heads_dev)
        kv = d * heads_dev // head_group
        out_ref[d, 0, :, 0:HEAD_DIMENSION] = full[rows, kv * HEAD_DIMENSION:(kv + 1) * HEAD_DIMENSION]
        out_ref[d, 0, :, HEAD_DIMENSION:2 * HEAD_DIMENSION] = peak_lanes[rows, :]
        out_ref[d, 0, :, 2 * HEAD_DIMENSION:] = total_lanes[rows, :]


def attention(heads_all, selected, limit, base, key_cache, value_store_cache, scale, head_group):
    requests, nseq, local_width = heads_all.shape
    heads_dev = local_width // HEAD_DIMENSION
    q_heads = nseq * heads_dev
    tok, width = key_cache.shape[1:]
    kernel = functools.partial(attention_kernel, scale=scale, head_group=head_group)
    flops = 4 * requests * q_heads * tok * width
    nbytes = 2 * (key_cache.size + value_store_cache.size + heads_all.size)
    return pl.pallas_call(
        kernel,
        grid=(requests,),
        in_specs=[
            pl.BlockSpec(memory_space=pltpu.SMEM),
            pl.BlockSpec(memory_space=pltpu.SMEM),
            pl.BlockSpec(memory_space=pltpu.SMEM),
            pl.BlockSpec((1, nseq, local_width), lambda r: (r, 0, 0)),
            pl.BlockSpec((1, tok, width), lambda r: (r, 0, 0)),
            pl.BlockSpec((1, tok, width), lambda r: (r, 0, 0)),
        ],
        out_specs=pl.BlockSpec((nseq, 1, heads_dev, 3 * HEAD_DIMENSION), lambda r: (0, r, 0, 0)),
        out_shape=jax.ShapeDtypeStruct((nseq, requests, heads_dev, 3 * HEAD_DIMENSION), jnp.float32),
        scratch_shapes=[pltpu.VMEM((q_heads, width), jnp.float32)],
        cost_estimate=pl.CostEstimate(
            flops=flops, transcendentals=requests * q_heads * tok, bytes_accessed=nbytes
        ),
    )(selected, limit, base, heads_all, key_cache, value_store_cache)


def body(query, key_cache, value_store_cache, selected, lengths, w_out):
    nseq = lax.axis_size("seq")
    me = lax.axis_index("seq")
    requests = query.shape[0]
    tok_local = key_cache.shape[1]
    kv_heads = key_cache.shape[2] // HEAD_DIMENSION
    heads_dev = query.shape[1] // HEAD_DIMENSION
    q_heads = heads_dev * nseq
    head_group = q_heads // kv_heads
    scale = HEAD_DIMENSION ** (-0.5)

    heads_all = lax.all_to_all(
        jnp.broadcast_to(query[:, None, :], (requests, nseq, query.shape[1])), "seq", 1, 1, tiled=True
    )

    limit = (lengths - me * tok_local).astype(jnp.int32)
    base = jnp.reshape(me * (tok_local // PAGE), (1,)).astype(jnp.int32)
    packed = attention(heads_all, selected, limit, base, key_cache, value_store_cache, scale, head_group)
    parts = lax.all_to_all(packed, "seq", 0, 0, tiled=True)
    b_out = parts[..., :HEAD_DIMENSION]
    b_max = parts[..., HEAD_DIMENSION:2 * HEAD_DIMENSION]
    b_sum = parts[..., 2 * HEAD_DIMENSION:]
    top = jnp.max(b_max, axis=0)
    factor = jnp.exp(b_max - top[None])
    whole_total = jnp.sum(b_sum * factor, axis=0)
    whole_accum = jnp.sum(b_out * factor, axis=0)
    attended = (
        (whole_accum / whole_total)
        .reshape(requests, heads_dev * HEAD_DIMENSION)
        .astype(jnp.bfloat16)
    )
    everyone = gather_by_all_to_all(attended, "grp").reshape(-1, attended.shape[1])
    partial = jnp.dot(everyone, w_out, preferred_element_type=jnp.float32)
    rows_out, cols_out = partial.shape[0] // nseq, partial.shape[1]
    partial = partial.reshape(nseq, -1, HEAD_DIMENSION)
    pieces = lax.all_to_all(partial, "seq", 0, 0, tiled=True)
    projected = jnp.sum(pieces, axis=0).reshape(rows_out, cols_out).astype(jnp.bfloat16)
    return (attended, projected)


def solution(mesh):
    return jax.shard_map(
        body,
        mesh=mesh,
        in_specs=(
            P("grp", "seq"),
            P("grp", "seq", None),
            P("grp", "seq", None),
            P("grp", None),
            P("grp"),
            P("seq", "grp"),
        ),
        out_specs=(P("grp", "seq"), P("seq", "grp")),
        check_vma=False,
    )
```

```python
import functools

import jax
import jax.numpy as jnp
from jax import lax
from jax.experimental import pallas as pl
from jax.experimental.pallas import tpu as pltpu
from jax.sharding import PartitionSpec as P

HEAD_DIMENSION = 128
PAGE = 64


NEG = -1e30


def gather_by_all_to_all(x, axis):
    n = lax.axis_size(axis)
    return lax.all_to_all(jnp.broadcast_to(x[None], (n,) + x.shape), axis, 0, 0, tiled=True)


def attention_kernel(sel_ref, lim_ref, base_ref, h_ref, k_ref, v_ref, out_ref, qd_ref, *, scale, head_group):
    _, nseq, local_width = h_ref.shape
    heads_dev = local_width // HEAD_DIMENSION
    tok, cols = k_ref.shape[1:]
    kv_step = cols // HEAD_DIMENSION
    heads_step = kv_step * head_group
    src_step = heads_step // heads_dev
    r = pl.program_id(0)
    c = pl.program_id(1)
    lane = lax.broadcasted_iota(jnp.int32, (1, tok), 1)
    page = base_ref[0] + lane // PAGE
    picked = page == sel_ref[r, 0]
    for j in range(1, sel_ref.shape[1]):
        picked = picked | (page == sel_ref[r, j])
    live = picked & (lane < lim_ref[r])
    for chunk in range(nseq // src_step):
        @pl.when(c == chunk)
        def _():
            qd_ref[...] = jnp.zeros(qd_ref.shape, qd_ref.dtype)
            for s_local in range(src_step):
                src = chunk * src_step + s_local
                for i in range(heads_dev):
                    h = s_local * heads_dev + i
                    kv = h // head_group
                    qd_ref[h:h + 1, kv * HEAD_DIMENSION:(kv + 1) * HEAD_DIMENSION] = h_ref[
                        0, src:src + 1, i * HEAD_DIMENSION:(i + 1) * HEAD_DIMENSION
                    ].astype(qd_ref.dtype)

    q = qd_ref[...].astype(jnp.bfloat16)
    scores = lax.dot_general(
        q, k_ref[0], (((1,), (1,)), ((), ())), preferred_element_type=jnp.float32
    ) * scale
    scores = jnp.where(live, scores, NEG)
    peak = jnp.max(scores, axis=-1, keepdims=True)
    weights = jnp.where(live, jnp.exp(scores - peak), 0.0)
    total = jnp.sum(weights, axis=-1, keepdims=True)
    full = jnp.dot(weights.astype(jnp.bfloat16), v_ref[0], preferred_element_type=jnp.float32)
    peak_lanes = jnp.broadcast_to(peak, (heads_step, HEAD_DIMENSION))
    total_lanes = jnp.broadcast_to(total, (heads_step, HEAD_DIMENSION))
    for d in range(src_step):
        rows = slice(d * heads_dev, (d + 1) * heads_dev)
        kv = d * heads_dev // head_group
        out_ref[d, 0, :, 0:HEAD_DIMENSION] = full[rows, kv * HEAD_DIMENSION:(kv + 1) * HEAD_DIMENSION]
        out_ref[d, 0, :, HEAD_DIMENSION:2 * HEAD_DIMENSION] = peak_lanes[rows, :]
        out_ref[d, 0, :, 2 * HEAD_DIMENSION:] = total_lanes[rows, :]


def attention(heads_all, selected, limit, base, key_cache, value_store_cache, scale, head_group, steps=2):
    requests, nseq, local_width = heads_all.shape
    heads_dev = local_width // HEAD_DIMENSION
    q_heads = nseq * heads_dev
    tok, width = key_cache.shape[1:]
    cols = width // steps
    heads_step = q_heads // steps
    src_step = nseq // steps
    kernel = functools.partial(attention_kernel, scale=scale, head_group=head_group)
    flops = 4 * requests * q_heads * tok * cols
    nbytes = 2 * (key_cache.size + value_store_cache.size + heads_all.size)
    smem = pl.BlockSpec(memory_space=pltpu.SMEM)
    return pl.pallas_call(
        kernel,
        grid=(requests, steps),
        in_specs=[
            smem,
            smem,
            smem,
            pl.BlockSpec((1, nseq, local_width), lambda r, c: (r, 0, 0)),
            pl.BlockSpec((1, tok, cols), lambda r, c: (r, 0, c)),
            pl.BlockSpec((1, tok, cols), lambda r, c: (r, 0, c)),
        ],
        out_specs=pl.BlockSpec((src_step, 1, heads_dev, 3 * HEAD_DIMENSION), lambda r, c: (c, r, 0, 0)),
        out_shape=jax.ShapeDtypeStruct((nseq, requests, heads_dev, 3 * HEAD_DIMENSION), jnp.float32),
        scratch_shapes=[pltpu.VMEM((heads_step, cols), jnp.float32)],
        cost_estimate=pl.CostEstimate(
            flops=flops, transcendentals=requests * q_heads * tok, bytes_accessed=nbytes
        ),
    )(selected, limit, base, heads_all, key_cache, value_store_cache)


def body(query, key_cache, value_store_cache, selected, lengths, w_out):
    nseq = lax.axis_size("seq")
    me = lax.axis_index("seq")
    requests = query.shape[0]
    tok_local = key_cache.shape[1]
    kv_heads = key_cache.shape[2] // HEAD_DIMENSION
    heads_dev = query.shape[1] // HEAD_DIMENSION
    q_heads = heads_dev * nseq
    head_group = q_heads // kv_heads
    scale = HEAD_DIMENSION ** (-0.5)

    heads_all = lax.all_to_all(
        jnp.broadcast_to(query[:, None, :], (requests, nseq, query.shape[1])), "seq", 1, 1, tiled=True
    )

    limit = (lengths - me * tok_local).astype(jnp.int32)
    base = jnp.reshape(me * (tok_local // PAGE), (1,)).astype(jnp.int32)
    packed = attention(heads_all, selected, limit, base, key_cache, value_store_cache, scale, head_group)
    parts = lax.all_to_all(packed, "seq", 0, 0, tiled=True)
    b_out = parts[..., :HEAD_DIMENSION]
    b_max = parts[..., HEAD_DIMENSION:2 * HEAD_DIMENSION]
    b_sum = parts[..., 2 * HEAD_DIMENSION:]
    top = jnp.max(b_max, axis=0)
    factor = jnp.exp(b_max - top[None])
    whole_total = jnp.sum(b_sum * factor, axis=0)
    whole_accum = jnp.sum(b_out * factor, axis=0)
    attended = (
        (whole_accum / whole_total)
        .reshape(requests, heads_dev * HEAD_DIMENSION)
        .astype(jnp.bfloat16)
    )
    everyone = gather_by_all_to_all(attended, "grp").reshape(-1, attended.shape[1])
    partial = jnp.dot(everyone, w_out, preferred_element_type=jnp.float32)
    rows_out, cols_out = partial.shape[0] // nseq, partial.shape[1]
    partial = partial.reshape(nseq, -1, HEAD_DIMENSION)
    pieces = lax.all_to_all(partial, "seq", 0, 0, tiled=True)
    projected = jnp.sum(pieces, axis=0).reshape(rows_out, cols_out).astype(jnp.bfloat16)
    return (attended, projected)


def solution(mesh):
    return jax.shard_map(
        body,
        mesh=mesh,
        in_specs=(
            P("grp", "seq"),
            P("grp", "seq", None),
            P("grp", "seq", None),
            P("grp", None),
            P("grp"),
            P("seq", "grp"),
        ),
        out_specs=(P("grp", "seq"), P("seq", "grp")),
        check_vma=False,
    )
```

```python
import functools

import jax
import jax.numpy as jnp
from jax import lax
from jax.experimental import pallas as pl
from jax.experimental.pallas import tpu as pltpu
from jax.sharding import PartitionSpec as P

HEAD_DIMENSION = 128
PAGE = 64


NEG = -1e30


def gather_by_all_to_all(x, axis):
    n = lax.axis_size(axis)
    return lax.all_to_all(jnp.broadcast_to(x[None], (n,) + x.shape), axis, 0, 0, tiled=True)


def attention_kernel(sel_ref, lim_ref, base_ref, h_ref, k_ref, v_ref, out_ref, qd_ref, *, scale, head_group):
    _, nseq, local_width = h_ref.shape
    heads_dev = local_width // HEAD_DIMENSION
    q_heads = nseq * heads_dev
    qd_ref[...] = jnp.zeros(qd_ref.shape, qd_ref.dtype)
    for src in range(nseq):
        for i in range(heads_dev):
            h = src * heads_dev + i
            kv = h // head_group
            qd_ref[h:h + 1, kv * HEAD_DIMENSION:(kv + 1) * HEAD_DIMENSION] = h_ref[
                0, src:src + 1, i * HEAD_DIMENSION:(i + 1) * HEAD_DIMENSION
            ].astype(qd_ref.dtype)
    q = qd_ref[...].astype(jnp.bfloat16)
    r = pl.program_id(0)
    tok = k_ref.shape[1]
    lane = lax.broadcasted_iota(jnp.int32, (1, tok), 1)
    page = base_ref[0] + lane // PAGE
    picked = page == sel_ref[r, 0]
    for j in range(1, sel_ref.shape[1]):
        picked = picked | (page == sel_ref[r, j])
    live = picked & (lane < lim_ref[r])
    scores = lax.dot_general(
        q, k_ref[0], (((1,), (1,)), ((), ())), preferred_element_type=jnp.float32
    ) * scale
    scores = jnp.where(live, scores, NEG)
    peak = jnp.max(scores, axis=-1, keepdims=True)
    weights = jnp.where(live, jnp.exp(scores - peak), 0.0)
    total = jnp.sum(weights, axis=-1, keepdims=True)
    full = jnp.dot(weights.astype(jnp.bfloat16), v_ref[0], preferred_element_type=jnp.float32)
    half = HEAD_DIMENSION // 2
    stat_lane = lax.broadcasted_iota(jnp.int32, (q_heads, HEAD_DIMENSION), 1)
    stat = jnp.where(stat_lane < half, peak, total)
    for d in range(nseq):
        rows = slice(d * heads_dev, (d + 1) * heads_dev)
        kv = d * heads_dev // head_group
        out_ref[d, 0, :, 0:HEAD_DIMENSION] = full[rows, kv * HEAD_DIMENSION:(kv + 1) * HEAD_DIMENSION]
        out_ref[d, 0, :, HEAD_DIMENSION:] = stat[rows, :]


def attention(heads_all, selected, limit, base, key_cache, value_store_cache, scale, head_group):
    requests, nseq, local_width = heads_all.shape
    heads_dev = local_width // HEAD_DIMENSION
    q_heads = nseq * heads_dev
    tok, width = key_cache.shape[1:]
    kernel = functools.partial(attention_kernel, scale=scale, head_group=head_group)
    flops = 4 * requests * q_heads * tok * width
    nbytes = 2 * (key_cache.size + value_store_cache.size + heads_all.size)
    return pl.pallas_call(
        kernel,
        grid=(requests,),
        in_specs=[
            pl.BlockSpec(memory_space=pltpu.SMEM),
            pl.BlockSpec(memory_space=pltpu.SMEM),
            pl.BlockSpec(memory_space=pltpu.SMEM),
            pl.BlockSpec((1, nseq, local_width), lambda r: (r, 0, 0)),
            pl.BlockSpec((1, tok, width), lambda r: (r, 0, 0)),
            pl.BlockSpec((1, tok, width), lambda r: (r, 0, 0)),
        ],
        out_specs=pl.BlockSpec((nseq, 1, heads_dev, 2 * HEAD_DIMENSION), lambda r: (0, r, 0, 0)),
        out_shape=jax.ShapeDtypeStruct((nseq, requests, heads_dev, 2 * HEAD_DIMENSION), jnp.float32),
        scratch_shapes=[pltpu.VMEM((q_heads, width), jnp.float32)],
        cost_estimate=pl.CostEstimate(
            flops=flops, transcendentals=requests * q_heads * tok, bytes_accessed=nbytes
        ),
    )(selected, limit, base, heads_all, key_cache, value_store_cache)


def body(query, key_cache, value_store_cache, selected, lengths, w_out):
    nseq = lax.axis_size("seq")
    me = lax.axis_index("seq")
    requests = query.shape[0]
    tok_local = key_cache.shape[1]
    kv_heads = key_cache.shape[2] // HEAD_DIMENSION
    heads_dev = query.shape[1] // HEAD_DIMENSION
    q_heads = heads_dev * nseq
    head_group = q_heads // kv_heads
    scale = HEAD_DIMENSION ** (-0.5)

    heads_all = lax.all_to_all(
        jnp.broadcast_to(query[:, None, :], (requests, nseq, query.shape[1])), "seq", 1, 1, tiled=True
    )

    limit = (lengths - me * tok_local).astype(jnp.int32)
    base = jnp.reshape(me * (tok_local // PAGE), (1,)).astype(jnp.int32)
    packed = attention(heads_all, selected, limit, base, key_cache, value_store_cache, scale, head_group)
    parts = lax.all_to_all(packed, "seq", 0, 0, tiled=True)
    half = HEAD_DIMENSION // 2
    b_out = parts[..., :HEAD_DIMENSION]
    b_max = parts[..., HEAD_DIMENSION:HEAD_DIMENSION + half]
    b_sum = parts[..., HEAD_DIMENSION + half:]
    top = jnp.max(b_max, axis=0)
    factor = jnp.exp(b_max - top[None])
    whole_total = jnp.sum(b_sum * factor, axis=0)
    whole_total = jnp.concatenate([whole_total, whole_total], axis=-1)
    whole_accum = jnp.sum(b_out * jnp.concatenate([factor, factor], axis=-1), axis=0)
    attended = (
        (whole_accum / whole_total)
        .reshape(requests, heads_dev * HEAD_DIMENSION)
        .astype(jnp.bfloat16)
    )
    everyone = gather_by_all_to_all(attended, "grp").reshape(-1, attended.shape[1])
    partial = jnp.dot(everyone, w_out, preferred_element_type=jnp.float32)
    rows_out, cols_out = partial.shape[0] // nseq, partial.shape[1]
    partial = partial.reshape(nseq, -1, HEAD_DIMENSION)
    pieces = lax.all_to_all(partial, "seq", 0, 0, tiled=True)
    projected = jnp.sum(pieces, axis=0).reshape(rows_out, cols_out).astype(jnp.bfloat16)
    return (attended, projected)


def solution(mesh):
    return jax.shard_map(
        body,
        mesh=mesh,
        in_specs=(
            P("grp", "seq"),
            P("grp", "seq", None),
            P("grp", "seq", None),
            P("grp", None),
            P("grp"),
            P("seq", "grp"),
        ),
        out_specs=(P("grp", "seq"), P("seq", "grp")),
        check_vma=False,
    )
```
